256 devices in a mesh: section: 16 (over x, z_lo, core), dp: 16 (over z_hi, y).
Axes of the slice: x: 4, y: 4, z: 8 (z_hi: 4, z_lo: 2; z = z_hi * 2 + z_lo), core: 2. Of those that a mesh axis runs over, the one named last changes fastest.
Arguments:
- encoder_out: bfloat16 [2, 2, 256, 4096], P(None, None, 'dp', 'section'), may hold values from -6 to 6
- encoder_len: int32 [2, 2], replicated, may hold values from 1 to 2, as said below
- decoder_len: int32 [2, 2], replicated, may hold values from 1 to 2, as said below
- queries: bfloat16 [16, 2, 2, 256, 4096], P('section', None, None, None, 'dp'), may hold values from -40 to 40
- cotangent: bfloat16 [16, 2, 2, 256, 4096], P('section', None, None, None, 'dp'), may hold values from -6 to 6
- key_weight: bfloat16 [16, 4096, 4096], P('section', None, 'dp'), may hold values from -0.09375 to 0.09375
- value_weight: bfloat16 [16, 4096, 4096], P('section', None, 'dp'), may hold values from -0.09375 to 0.09375
Outputs:
- attention: bfloat16 [16, 2, 2, 256, 4096], P('section', None, None, None, 'dp')
- grad_query: bfloat16 [16, 2, 2, 256, 4096], P('section', None, None, None, 'dp')
- grad_key_weight: bfloat16 [16, 4096, 4096], P('section', None, 'dp')
- grad_value_weight: bfloat16 [16, 4096, 4096], P('section', None, 'dp')
- grad_encoder: float32 [2, 2, 256, 4096], P(None, None, 'dp', 'section')
The draws below stay inside these ranges and needn't reach their ends.
Inputs may be any that keep to these rules, and one draw needn't show every extreme that they name: `encoder_len`: in every micro-batch some example fills all 2 encoder blocks. `decoder_len`: in every micro-batch some example fills all 2 decoder blocks.
All inputs are finite; a program needn't handle non-finite values.
Results may differ from the reference program's by a relative error of at most 0.012.
The reference program's roundings to bfloat16 on the way count: a program that leaves them out, or rounds other values in their place, can miss the bound.
Values may be sent and summed in bfloat16 or wider, within the bound.
No kernel may reach another device: no remote copies, remote signals or barrier semaphores. Data moves between devices by JAX's collectives and lax.ppermute only.
A program may use at most 128 MiB of HBM per device.

```python
import jax
import jax.numpy as jnp
from jax import lax

D = 4096
HEADS = 16
HD = 256
INNER = 4096
BLOCK = 128
ENC_BLOCKS = 2
DEC_BLOCKS = 2
EX = 2
MICRO = 2
SECTIONS = 16


def length_table(key, blocks):
    picked = jax.random.randint(key, (MICRO, EX), 1, blocks + 1)
    fullest = jax.random.randint(jax.random.fold_in(key, 7), (MICRO, 1), 0, EX)
    return jnp.where(jnp.arange(EX)[None, :] == fullest, blocks, picked).astype(jnp.int32)


def draw_encoder_len(key, part):
    return length_table(jax.random.fold_in(key, 11), ENC_BLOCKS)


def draw_decoder_len(key, part):
    return length_table(jax.random.fold_in(key, 13), DEC_BLOCKS)


def draw_queries(key, part):
    shape = (SECTIONS, MICRO, EX, DEC_BLOCKS * BLOCK, INNER)
    base = jax.random.truncated_normal(jax.random.fold_in(key, 17), -4.0, 4.0, shape, jnp.float32)
    return base.astype(jnp.bfloat16)


def shard_levels(stream_key, shape, split, least, high):
    def one(position, parts):
        draws = jax.random.uniform(jax.random.fold_in(jax.random.fold_in(stream_key, 6), position), (parts,), jnp.float32, least / len(split), high / len(split))
        return jnp.repeat(jnp.exp(draws), shape[position] // parts).reshape((-1,) + (1,) * (len(shape) - position - 1))

    factor_of = one(*split[0])
    for cut in split[1:]:
        factor_of = factor_of * one(*cut)
    return factor_of


def scatter_about(rng, dims, scale, bound, pieces=(), held_as=jnp.bfloat16):
    array = jax.random.normal(rng, dims, jnp.float32) * scale
    if len(pieces) > 0:
        array = shard_levels(rng, dims, pieces, -0.22, 0.18) * array
    return jnp.clip(array, min=-bound, max=bound).astype(held_as)


def setup_inputs(seed: int = 0) -> dict:
    key_of = jax.random.split(jax.random.key(seed), 8)
    encoder_out = scatter_about(key_of[0], (MICRO, EX, ENC_BLOCKS * BLOCK, D), 1.0, 6.0, ((2, 16), (3, 16)))
    encoder_len = draw_encoder_len(jax.random.fold_in(key_of[7], 71), 0)
    decoder_len = draw_decoder_len(jax.random.fold_in(key_of[7], 71), 0)
    queries = draw_queries(jax.random.fold_in(key_of[7], 71), 0)
    cotangent = scatter_about(key_of[4], (SECTIONS, MICRO, EX, DEC_BLOCKS * BLOCK, INNER), 1.0, 6.0, ((0, 16), (4, 16)))
    key_weight = scatter_about(key_of[5], (SECTIONS, D, INNER), D ** -0.5, 0.09375, ((0, 16), (2, 16)))
    value_weight = scatter_about(key_of[6], (SECTIONS, D, INNER), D ** -0.5, 0.09375, ((0, 16), (2, 16)))
    return {"encoder_out": encoder_out, "encoder_len": encoder_len, "decoder_len": decoder_len, "queries": queries, "cotangent": cotangent, "key_weight": key_weight, "value_weight": value_weight}


NEG_FILL = -1e30


def attend(query_rows, key_rows, value_rows, cotan_rows, key_valid, query_valid):
    score_scale = HD ** -0.5
    query_float = query_rows.astype(jnp.float32)
    key_float = key_rows.astype(jnp.float32)
    value_float = value_rows.astype(jnp.float32)
    scores = jnp.einsum("eqhd,ekhd->ehqk", query_float, key_float) * score_scale
    scores = jnp.where(key_valid[:, None, None, :], scores, NEG_FILL)
    largest = jnp.max(scores, axis=-1, keepdims=True)
    weights = jnp.exp(scores - largest)
    probs = weights / jnp.sum(weights, axis=-1, keepdims=True)
    probs_low = lax.optimization_barrier(probs.astype(jnp.bfloat16)).astype(jnp.float32)
    attended = jnp.einsum("ehqk,ekhd->eqhd", probs_low, value_float)
    attended = jnp.where(query_valid[:, :, None, None], attended, 0.0).astype(jnp.bfloat16)
    cotan_float = jnp.where(query_valid[:, :, None, None], cotan_rows.astype(jnp.float32), 0.0)
    grad_value = jnp.einsum("ehqk,eqhd->ekhd", probs_low, cotan_float).astype(jnp.bfloat16)
    grad_probs = jnp.einsum("eqhd,ekhd->ehqk", cotan_float, value_float)
    inner_sum = jnp.sum(probs * grad_probs, axis=-1, keepdims=True)
    grad_scores = (probs * (grad_probs - inner_sum) * score_scale).astype(jnp.bfloat16)
    grad_scores = lax.optimization_barrier(grad_scores).astype(jnp.float32)
    grad_query = jnp.einsum("ehqk,ekhd->eqhd", grad_scores, key_float).astype(jnp.bfloat16)
    grad_key = jnp.einsum("ehqk,eqhd->ekhd", grad_scores, query_float).astype(jnp.bfloat16)
    return attended, grad_query, grad_key, grad_value


def reference(encoder_out, encoder_len, decoder_len, queries, cotangent, key_weight, value_weight):
    enc_rows = ENC_BLOCKS * BLOCK
    dec_rows = DEC_BLOCKS * BLOCK
    key_valid = jnp.arange(enc_rows, dtype=jnp.int32)[None, None, :] < (BLOCK * encoder_len)[:, :, None]
    query_valid = jnp.arange(dec_rows, dtype=jnp.int32)[None, None, :] < (BLOCK * decoder_len)[:, :, None]
    grad_encoder = jnp.zeros((MICRO, EX, enc_rows, D), jnp.float32)
    attn_all, query_all, key_all, value_all = [], [], [], []
    for section_idx in range(SECTIONS):
        key_mat = key_weight[section_idx].astype(jnp.float32)
        value_mat = value_weight[section_idx].astype(jnp.float32)
        key_acc = jnp.zeros((D, INNER), jnp.float32)
        value_acc = jnp.zeros((D, INNER), jnp.float32)
        attn_micro, query_micro = [], []
        for micro_idx in range(MICRO):
            encoder_float = encoder_out[micro_idx].astype(jnp.float32)
            key_rows = jnp.einsum("ekd,dc->ekc", encoder_float, key_mat).astype(jnp.bfloat16)
            value_rows = jnp.einsum("ekd,dc->ekc", encoder_float, value_mat).astype(jnp.bfloat16)
            attended, grad_query, grad_key, grad_value = attend(
                queries[section_idx, micro_idx].reshape(EX, dec_rows, HEADS, HD),
                key_rows.reshape(EX, enc_rows, HEADS, HD),
                value_rows.reshape(EX, enc_rows, HEADS, HD),
                cotangent[section_idx, micro_idx].reshape(EX, dec_rows, HEADS, HD),
                key_valid[micro_idx], query_valid[micro_idx])
            key_flat = grad_key.reshape(EX, enc_rows, INNER).astype(jnp.float32)
            value_flat = grad_value.reshape(EX, enc_rows, INNER).astype(jnp.float32)
            key_acc = key_acc + jnp.einsum("ekd,ekc->dc", encoder_float, key_flat)
            value_acc = value_acc + jnp.einsum("ekd,ekc->dc", encoder_float, value_flat)
            term = jnp.einsum("ekc,dc->ekd", key_flat, key_mat) + jnp.einsum("ekc,dc->ekd", value_flat, value_mat)
            grad_encoder = grad_encoder.at[micro_idx].add(term)
            attn_micro.append(attended.reshape(EX, dec_rows, INNER))
            query_micro.append(grad_query.reshape(EX, dec_rows, INNER))
        attn_all.append(jnp.stack(attn_micro))
        query_all.append(jnp.stack(query_micro))
        key_all.append(key_acc.astype(jnp.bfloat16))
        value_all.append(value_acc.astype(jnp.bfloat16))
    return (jnp.stack(attn_all), jnp.stack(query_all), jnp.stack(key_all), jnp.stack(value_all), grad_encoder)
```

```python
import jax
import jax.numpy as jnp
from jax import lax
from jax.sharding import PartitionSpec as P

HD = 256
BLOCK = 128
ENC_BLOCKS = 2
MICRO = 2


NEG_FILL = -1e30


def attend(query_rows, key_rows, value_rows, cotan_rows, key_valid, query_valid):
    score_scale = HD ** (-0.5)
    scores = (
        jnp.einsum("eqhd,ekhd->ehqk", query_rows, key_rows, preferred_element_type=jnp.float32)
        * score_scale
    )
    scores = jnp.where(key_valid[:, None, None, :], scores, NEG_FILL)
    largest = jnp.max(scores, axis=-1, keepdims=True)
    weights = jnp.exp(scores - largest)
    probs = weights / jnp.sum(weights, axis=-1, keepdims=True)
    probs_low = probs.astype(jnp.bfloat16)
    attended = jnp.einsum(
        "ehqk,ekhd->eqhd", probs_low, value_rows, preferred_element_type=jnp.float32
    )
    attended = jnp.where(query_valid[:, :, None, None], attended, 0.0).astype(jnp.bfloat16)
    cotan_kept = jnp.where(query_valid[:, :, None, None], cotan_rows, jnp.zeros_like(cotan_rows))
    grad_value = jnp.einsum(
        "ehqk,eqhd->ekhd", probs_low, cotan_kept, preferred_element_type=jnp.float32
    ).astype(jnp.bfloat16)
    grad_probs = jnp.einsum(
        "eqhd,ekhd->ehqk", cotan_kept, value_rows, preferred_element_type=jnp.float32
    )
    inner_sum = jnp.sum(probs * grad_probs, axis=-1, keepdims=True)
    grad_scores = (probs * (grad_probs - inner_sum) * score_scale).astype(jnp.bfloat16)
    grad_query = jnp.einsum(
        "ehqk,ekhd->eqhd", grad_scores, key_rows, preferred_element_type=jnp.float32
    ).astype(jnp.bfloat16)
    grad_key = jnp.einsum(
        "ehqk,eqhd->ekhd", grad_scores, query_rows, preferred_element_type=jnp.float32
    ).astype(jnp.bfloat16)
    return (attended, grad_query, grad_key, grad_value)


def body(encoder_out, encoder_len, decoder_len, queries, cotangent, key_weight, value_weight):
    key_mat = key_weight[0]
    value_mat = value_weight[0]
    width_dev = key_mat.shape[1]
    heads_dev = width_dev // HD
    enc_rows = ENC_BLOCKS * BLOCK
    dec_rows = queries.shape[3]
    examples = queries.shape[2]
    rows_dev = enc_rows // lax.axis_size("dp")
    key_positions = jnp.arange(enc_rows, dtype=jnp.int32)
    query_positions = jnp.arange(dec_rows, dtype=jnp.int32)
    key_acc = jnp.zeros(key_mat.shape, jnp.float32)
    value_acc = jnp.zeros(value_mat.shape, jnp.float32)
    attn_list, query_list, encoder_list = ([], [], [])
    tall_enc = lax.all_gather(encoder_out, "dp", axis=2, tiled=True)
    gathered_enc = lax.all_gather(tall_enc, "section", axis=3, tiled=True)
    for micro_idx in range(MICRO):
        whole_enc = gathered_enc[micro_idx]
        key_rows = jnp.einsum(
            "ekd,dc->ekc", whole_enc, key_mat, preferred_element_type=jnp.float32
        ).astype(jnp.bfloat16)
        value_rows = jnp.einsum(
            "ekd,dc->ekc", whole_enc, value_mat, preferred_element_type=jnp.float32
        ).astype(jnp.bfloat16)
        key_valid = key_positions[None, :] < (BLOCK * encoder_len[micro_idx])[:, None]
        query_valid = query_positions[None, :] < (BLOCK * decoder_len[micro_idx])[:, None]
        attended, grad_query, grad_key, grad_value = attend(
            queries[0, micro_idx].reshape(examples, dec_rows, heads_dev, HD),
            key_rows.reshape(examples, enc_rows, heads_dev, HD),
            value_rows.reshape(examples, enc_rows, heads_dev, HD),
            cotangent[0, micro_idx].reshape(examples, dec_rows, heads_dev, HD),
            key_valid,
            query_valid,
        )
        key_flat = grad_key.reshape(examples, enc_rows, width_dev)
        value_flat = grad_value.reshape(examples, enc_rows, width_dev)
        key_acc = key_acc + jnp.einsum(
            "ekd,ekc->dc", whole_enc, key_flat, preferred_element_type=jnp.float32
        )
        value_acc = value_acc + jnp.einsum(
            "ekd,ekc->dc", whole_enc, value_flat, preferred_element_type=jnp.float32
        )

        def head_term(first_row, row_count, key_flat=key_flat, value_flat=value_flat):
            return jnp.einsum(
                "ekc,dc->ked", key_flat, key_mat, preferred_element_type=jnp.float32
            ) + jnp.einsum("ekc,dc->ked", value_flat, value_mat, preferred_element_type=jnp.float32)

        encoder_list.append(head_term(jnp.int32(0), lax.axis_size("dp") * rows_dev))
        attn_list.append(attended.reshape(examples, dec_rows, width_dev))
        query_list.append(grad_query.reshape(examples, dec_rows, width_dev))
    attention = jnp.stack(attn_list)[None]
    query_grads = jnp.stack(query_list)[None]
    key_grads = key_acc.astype(jnp.bfloat16)[None]
    value_grads = value_acc.astype(jnp.bfloat16)[None]
    terms = jnp.stack(encoder_list)
    section_share = lax.psum_scatter(terms, "section", scatter_dimension=3, tiled=True)
    head_share = lax.psum_scatter(section_share, "dp", scatter_dimension=1, tiled=True)
    grad_encoder = jnp.transpose(head_share, (0, 2, 1, 3))
    return (attention, query_grads, key_grads, value_grads, grad_encoder)


def solution(mesh):
    placed = (
        P(None, None, "dp", "section"),
        P(),
        P(),
        P("section", None, None, None, "dp"),
        P("section", None, None, None, "dp"),
        P("section", None, "dp"),
        P("section", None, "dp"),
    )
    return jax.shard_map(
        body,
        mesh=mesh,
        in_specs=placed,
        out_specs=(
            P("section", None, None, None, "dp"),
            P("section", None, None, None, "dp"),
            P("section", None, "dp"),
            P("section", None, "dp"),
            P(None, None, "dp", "section"),
        ),
        check_vma=False,
    )
```

```python
import jax
import jax.numpy as jnp
from jax import lax
from jax.sharding import PartitionSpec as P

HD = 256
BLOCK = 128
ENC_BLOCKS = 2
MICRO = 2


NEG_FILL = -1e30


def attend(query_rows, key_rows, value_rows, cotan_rows, key_valid, query_valid):
    score_scale = HD ** (-0.5)
    scores = (
        jnp.einsum("eqhd,ekhd->ehqk", query_rows, key_rows, preferred_element_type=jnp.float32)
        * score_scale
    )
    scores = jnp.where(key_valid[:, None, None, :], scores, NEG_FILL)
    largest = jnp.max(scores, axis=-1, keepdims=True)
    weights = jnp.exp(scores - largest)
    probs = weights / jnp.sum(weights, axis=-1, keepdims=True)
    probs_low = probs.astype(jnp.bfloat16)
    attended = jnp.einsum(
        "ehqk,ekhd->eqhd", probs_low, value_rows, preferred_element_type=jnp.float32
    )
    attended = jnp.where(query_valid[:, :, None, None], attended, 0.0).astype(jnp.bfloat16)
    cotan_kept = jnp.where(query_valid[:, :, None, None], cotan_rows, jnp.zeros_like(cotan_rows))
    grad_value = jnp.einsum(
        "ehqk,eqhd->ekhd", probs_low, cotan_kept, preferred_element_type=jnp.float32
    ).astype(jnp.bfloat16)
    grad_probs = jnp.einsum(
        "eqhd,ekhd->ehqk", cotan_kept, value_rows, preferred_element_type=jnp.float32
    )
    inner_sum = jnp.sum(probs * grad_probs, axis=-1, keepdims=True)
    grad_scores = (probs * (grad_probs - inner_sum) * score_scale).astype(jnp.bfloat16)
    grad_query = jnp.einsum(
        "ehqk,ekhd->eqhd", grad_scores, key_rows, preferred_element_type=jnp.float32
    ).astype(jnp.bfloat16)
    grad_key = jnp.einsum(
        "ehqk,eqhd->ekhd", grad_scores, query_rows, preferred_element_type=jnp.float32
    ).astype(jnp.bfloat16)
    return (attended, grad_query, grad_key, grad_value)


def body(encoder_out, encoder_len, decoder_len, queries, cotangent, key_weight, value_weight):
    key_mat = key_weight[0]
    value_mat = value_weight[0]
    width_dev = key_mat.shape[1]
    heads_dev = width_dev // HD
    enc_rows = ENC_BLOCKS * BLOCK
    dec_rows = queries.shape[3]
    examples = queries.shape[2]
    rows_dev = enc_rows // lax.axis_size("dp")
    key_positions = jnp.arange(enc_rows, dtype=jnp.int32)
    query_positions = jnp.arange(dec_rows, dtype=jnp.int32)
    key_acc = jnp.zeros(key_mat.shape, jnp.float32)
    value_acc = jnp.zeros(value_mat.shape, jnp.float32)
    attn_list, query_list, encoder_list = ([], [], [])
    tall_enc = lax.all_gather(encoder_out, "dp", axis=2, tiled=True)
    gathered_enc = lax.all_gather(tall_enc, "section", axis=3, tiled=True)
    for micro_idx in range(MICRO):
        whole_enc = gathered_enc[micro_idx]
        key_rows = jnp.einsum(
            "ekd,dc->ekc", whole_enc, key_mat, preferred_element_type=jnp.float32
        ).astype(jnp.bfloat16)
        value_rows = jnp.einsum(
            "ekd,dc->ekc", whole_enc, value_mat, preferred_element_type=jnp.float32
        ).astype(jnp.bfloat16)
        key_valid = key_positions[None, :] < (BLOCK * encoder_len[micro_idx])[:, None]
        query_valid = query_positions[None, :] < (BLOCK * decoder_len[micro_idx])[:, None]
        attended, grad_query, grad_key, grad_value = attend(
            queries[0, micro_idx].reshape(examples, dec_rows, heads_dev, HD),
            key_rows.reshape(examples, enc_rows, heads_dev, HD),
            value_rows.reshape(examples, enc_rows, heads_dev, HD),
            cotangent[0, micro_idx].reshape(examples, dec_rows, heads_dev, HD),
            key_valid,
            query_valid,
        )
        key_flat = grad_key.reshape(examples, enc_rows, width_dev)
        value_flat = grad_value.reshape(examples, enc_rows, width_dev)
        key_acc = key_acc + jnp.einsum(
            "ekd,ekc->dc", whole_enc, key_flat, preferred_element_type=jnp.float32
        )
        value_acc = value_acc + jnp.einsum(
            "ekd,ekc->dc", whole_enc, value_flat, preferred_element_type=jnp.float32
        )

        def head_term(first_row, row_count, key_flat=key_flat, value_flat=value_flat):
            return jnp.einsum(
                "ekc,dc->ked", key_flat, key_mat, preferred_element_type=jnp.float32
            ) + jnp.einsum("ekc,dc->ked", value_flat, value_mat, preferred_element_type=jnp.float32)

        encoder_list.append(head_term(jnp.int32(0), lax.axis_size("dp") * rows_dev))
        attn_list.append(attended.reshape(examples, dec_rows, width_dev))
        query_list.append(grad_query.reshape(examples, dec_rows, width_dev))
    attention = jnp.stack(attn_list)[None]
    query_grads = jnp.stack(query_list)[None]
    key_grads = key_acc.astype(jnp.bfloat16)[None]
    value_grads = value_acc.astype(jnp.bfloat16)[None]
    terms = jnp.stack(encoder_list).astype(jnp.bfloat16)
    section_share = lax.psum_scatter(terms, "section", scatter_dimension=3, tiled=True)
    section_share = section_share.astype(jnp.float32)
    head_share = lax.psum_scatter(section_share, "dp", scatter_dimension=1, tiled=True)
    grad_encoder = jnp.transpose(head_share, (0, 2, 1, 3))
    return (attention, query_grads, key_grads, value_grads, grad_encoder)


def solution(mesh):
    placed = (
        P(None, None, "dp", "section"),
        P(),
        P(),
        P("section", None, None, None, "dp"),
        P("section", None, None, None, "dp"),
        P("section", None, "dp"),
        P("section", None, "dp"),
    )
    return jax.shard_map(
        body,
        mesh=mesh,
        in_specs=placed,
        out_specs=(
            P("section", None, None, None, "dp"),
            P("section", None, None, None, "dp"),
            P("section", None, "dp"),
            P("section", None, "dp"),
            P(None, None, "dp", "section"),
        ),
        check_vma=False,
    )
```

```python
import jax
import jax.numpy as jnp
from jax import lax
from jax.sharding import PartitionSpec as P

HD = 256
BLOCK = 128
ENC_BLOCKS = 2
MICRO = 2


NEG_FILL = -1e30


def attend(query_rows, key_rows, value_rows, cotan_rows, key_valid, query_valid):
    score_scale = HD ** (-0.5)
    scores = (
        jnp.einsum("eqhd,ekhd->ehqk", query_rows, key_rows, preferred_element_type=jnp.float32)
        * score_scale
    )
    scores = jnp.where(key_valid[:, None, None, :], scores, NEG_FILL)
    largest = jnp.max(scores, axis=-1, keepdims=True)
    weights = jnp.exp(scores - largest)
    probs = weights / jnp.sum(weights, axis=-1, keepdims=True)
    probs_low = probs.astype(jnp.bfloat16)
    attended = jnp.einsum(
        "ehqk,ekhd->eqhd", probs_low, value_rows, preferred_element_type=jnp.float32
    )
    attended = jnp.where(query_valid[:, :, None, None], attended, 0.0).astype(jnp.bfloat16)
    cotan_kept = jnp.where(query_valid[:, :, None, None], cotan_rows, jnp.zeros_like(cotan_rows))
    grad_value = jnp.einsum(
        "ehqk,eqhd->ekhd", probs_low, cotan_kept, preferred_element_type=jnp.float32
    ).astype(jnp.bfloat16)
    grad_probs = jnp.einsum(
        "eqhd,ekhd->ehqk", cotan_kept, value_rows, preferred_element_type=jnp.float32
    )
    inner_sum = jnp.sum(probs * grad_probs, axis=-1, keepdims=True)
    grad_scores = (probs * (grad_probs - inner_sum) * score_scale).astype(jnp.bfloat16)
    grad_query = jnp.einsum(
        "ehqk,ekhd->eqhd", grad_scores, key_rows, preferred_element_type=jnp.float32
    ).astype(jnp.bfloat16)
    grad_key = jnp.einsum(
        "ehqk,eqhd->ekhd", grad_scores, query_rows, preferred_element_type=jnp.float32
    ).astype(jnp.bfloat16)
    return (attended, grad_query, grad_key, grad_value)


def body(encoder_out, encoder_len, decoder_len, queries, cotangent, key_weight, value_weight):
    key_mat = key_weight[0]
    value_mat = value_weight[0]
    width_dev = key_mat.shape[1]
    heads_dev = width_dev // HD
    enc_rows = ENC_BLOCKS * BLOCK
    dec_rows = queries.shape[3]
    examples = queries.shape[2]
    rows_dev = enc_rows // lax.axis_size("dp")
    key_positions = jnp.arange(enc_rows, dtype=jnp.int32)
    query_positions = jnp.arange(dec_rows, dtype=jnp.int32)
    key_acc = jnp.zeros(key_mat.shape, jnp.float32)
    value_acc = jnp.zeros(value_mat.shape, jnp.float32)
    attn_list, query_list, encoder_list = ([], [], [])
    tall_enc = lax.all_gather(encoder_out, "dp", axis=2, tiled=True)
    gathered_enc = lax.all_gather(tall_enc, "section", axis=3, tiled=True)
    for micro_idx in range(MICRO):
        whole_enc = gathered_enc[micro_idx]
        key_rows = jnp.einsum(
            "ekd,dc->ekc", whole_enc, key_mat, preferred_element_type=jnp.float32
        ).astype(jnp.bfloat16)
        value_rows = jnp.einsum(
            "ekd,dc->ekc", whole_enc, value_mat, preferred_element_type=jnp.float32
        ).astype(jnp.bfloat16)
        key_valid = key_positions[None, :] < (BLOCK * encoder_len[micro_idx])[:, None]
        query_valid = query_positions[None, :] < (BLOCK * decoder_len[micro_idx])[:, None]
        attended, grad_query, grad_key, grad_value = attend(
            queries[0, micro_idx].reshape(examples, dec_rows, heads_dev, HD),
            key_rows.reshape(examples, enc_rows, heads_dev, HD),
            value_rows.reshape(examples, enc_rows, heads_dev, HD),
            cotangent[0, micro_idx].reshape(examples, dec_rows, heads_dev, HD),
            key_valid,
            query_valid,
        )
        key_flat = grad_key.reshape(examples, enc_rows, width_dev)
        value_flat = grad_value.reshape(examples, enc_rows, width_dev)
        key_acc = key_acc + jnp.einsum(
            "ekd,ekc->dc", whole_enc, key_flat, preferred_element_type=jnp.float32
        )
        value_acc = value_acc + jnp.einsum(
            "ekd,ekc->dc", whole_enc, value_flat, preferred_element_type=jnp.float32
        )

        def head_term(first_row, row_count, key_flat=key_flat, value_flat=value_flat):
            return jnp.einsum(
                "ekc,dc->ked", key_flat, key_mat, preferred_element_type=jnp.float32
            ) + jnp.einsum("ekc,dc->ked", value_flat, value_mat, preferred_element_type=jnp.float32)

        encoder_list.append(head_term(jnp.int32(0), lax.axis_size("dp") * rows_dev))
        attn_list.append(attended.reshape(examples, dec_rows, width_dev))
        query_list.append(grad_query.reshape(examples, dec_rows, width_dev))
    attention = jnp.stack(attn_list)[None]
    query_grads = jnp.stack(query_list)[None]
    key_grads = key_acc.astype(jnp.bfloat16)[None]
    value_grads = value_acc.astype(jnp.bfloat16)[None]
    terms = jnp.stack(encoder_list).astype(jnp.bfloat16)
    section_share = lax.psum_scatter(terms, "section", scatter_dimension=3, tiled=True)
    section_share = section_share.astype(jnp.float32)
    micro, enc_rows_all, examples_all, width_sec = section_share.shape
    groups = lax.axis_size("dp")
    row_blocks = section_share.reshape(
        micro, groups, enc_rows_all // groups, examples_all, width_sec
    ).transpose(1, 0, 3, 2, 4)
    received = lax.all_to_all(row_blocks, "dp", 0, 0, tiled=True)
    grad_encoder = jnp.sum(received, axis=0)
    return (attention, query_grads, key_grads, value_grads, grad_encoder)


def solution(mesh):
    placed = (
        P(None, None, "dp", "section"),
        P(),
        P(),
        P("section", None, None, None, "dp"),
        P("section", None, None, None, "dp"),
        P("section", None, "dp"),
        P("section", None, "dp"),
    )
    return jax.shard_map(
        body,
        mesh=mesh,
        in_specs=placed,
        out_specs=(
            P("section", None, None, None, "dp"),
            P("section", None, None, None, "dp"),
            P("section", None, "dp"),
            P("section", None, "dp"),
            P(None, None, "dp", "section"),
        ),
        check_vma=False,
    )
```

```python
import jax
import jax.numpy as jnp
from jax import lax
from jax.sharding import PartitionSpec as P

HD = 256
BLOCK = 128
ENC_BLOCKS = 2
MICRO = 2


NEG_FILL = -1e30


def attend(query_rows, key_rows, value_rows, cotan_rows, key_valid, query_valid):
    score_scale = HD ** (-0.5)
    scores = (
        jnp.einsum("eqhd,ekhd->ehqk", query_rows, key_rows, preferred_element_type=jnp.float32)
        * score_scale
    )
    scores = jnp.where(key_valid[:, None, None, :], scores, NEG_FILL)
    largest = jnp.max(scores, axis=-1, keepdims=True)
    weights = jnp.exp(scores - largest)
    probs = weights / jnp.sum(weights, axis=-1, keepdims=True)
    probs_low = probs.astype(jnp.bfloat16)
    attended = jnp.einsum(
        "ehqk,ekhd->eqhd", probs_low, value_rows, preferred_element_type=jnp.float32
    )
    attended = jnp.where(query_valid[:, :, None, None], attended, 0.0).astype(jnp.bfloat16)
    cotan_kept = jnp.where(query_valid[:, :, None, None], cotan_rows, jnp.zeros_like(cotan_rows))
    grad_value = jnp.einsum(
        "ehqk,eqhd->ekhd", probs_low, cotan_kept, preferred_element_type=jnp.float32
    ).astype(jnp.bfloat16)
    grad_probs = jnp.einsum(
        "eqhd,ekhd->ehqk", cotan_kept, value_rows, preferred_element_type=jnp.float32
    )
    inner_sum = jnp.sum(probs * grad_probs, axis=-1, keepdims=True)
    grad_scores = (probs * (grad_probs - inner_sum) * score_scale).astype(jnp.bfloat16)
    grad_query = jnp.einsum(
        "ehqk,ekhd->eqhd", grad_scores, key_rows, preferred_element_type=jnp.float32
    ).astype(jnp.bfloat16)
    grad_key = jnp.einsum(
        "ehqk,eqhd->ekhd", grad_scores, query_rows, preferred_element_type=jnp.float32
    ).astype(jnp.bfloat16)
    return (attended, grad_query, grad_key, grad_value)


def body(encoder_out, encoder_len, decoder_len, queries, cotangent, key_weight, value_weight):
    key_mat = key_weight[0]
    value_mat = value_weight[0]
    width_dev = key_mat.shape[1]
    heads_dev = width_dev // HD
    enc_rows = ENC_BLOCKS * BLOCK
    dec_rows = queries.shape[3]
    examples = queries.shape[2]
    rows_dev = enc_rows // lax.axis_size("dp")
    key_positions = jnp.arange(enc_rows, dtype=jnp.int32)
    query_positions = jnp.arange(dec_rows, dtype=jnp.int32)
    key_acc = jnp.zeros(key_mat.shape, jnp.float32)
    value_acc = jnp.zeros(value_mat.shape, jnp.float32)
    attn_list, query_list, encoder_list = ([], [], [])
    groups = lax.axis_size("dp")
    copies = jnp.broadcast_to(encoder_out[None], (groups,) + encoder_out.shape)
    from_each = lax.all_to_all(copies, "dp", 0, 0, tiled=True)
    tall_enc = jnp.moveaxis(from_each, 0, 2).reshape(
        encoder_out.shape[:2] + (groups * encoder_out.shape[2], encoder_out.shape[3])
    )
    gathered_enc = lax.all_gather(tall_enc, "section", axis=3, tiled=True)
    for micro_idx in range(MICRO):
        whole_enc = gathered_enc[micro_idx]
        key_rows = jnp.einsum(
            "ekd,dc->ekc", whole_enc, key_mat, preferred_element_type=jnp.float32
        ).astype(jnp.bfloat16)
        value_rows = jnp.einsum(
            "ekd,dc->ekc", whole_enc, value_mat, preferred_element_type=jnp.float32
        ).astype(jnp.bfloat16)
        key_valid = key_positions[None, :] < (BLOCK * encoder_len[micro_idx])[:, None]
        query_valid = query_positions[None, :] < (BLOCK * decoder_len[micro_idx])[:, None]
        attended, grad_query, grad_key, grad_value = attend(
            queries[0, micro_idx].reshape(examples, dec_rows, heads_dev, HD),
            key_rows.reshape(examples, enc_rows, heads_dev, HD),
            value_rows.reshape(examples, enc_rows, heads_dev, HD),
            cotangent[0, micro_idx].reshape(examples, dec_rows, heads_dev, HD),
            key_valid,
            query_valid,
        )
        key_flat = grad_key.reshape(examples, enc_rows, width_dev)
        value_flat = grad_value.reshape(examples, enc_rows, width_dev)
        key_acc = key_acc + jnp.einsum(
            "ekd,ekc->dc", whole_enc, key_flat, preferred_element_type=jnp.float32
        )
        value_acc = value_acc + jnp.einsum(
            "ekd,ekc->dc", whole_enc, value_flat, preferred_element_type=jnp.float32
        )

        def head_term(first_row, row_count, key_flat=key_flat, value_flat=value_flat):
            return jnp.einsum(
                "ekc,dc->ked", key_flat, key_mat, preferred_element_type=jnp.float32
            ) + jnp.einsum("ekc,dc->ked", value_flat, value_mat, preferred_element_type=jnp.float32)

        encoder_list.append(head_term(jnp.int32(0), lax.axis_size("dp") * rows_dev))
        attn_list.append(attended.reshape(examples, dec_rows, width_dev))
        query_list.append(grad_query.reshape(examples, dec_rows, width_dev))
    attention = jnp.stack(attn_list)[None]
    query_grads = jnp.stack(query_list)[None]
    key_grads = key_acc.astype(jnp.bfloat16)[None]
    value_grads = value_acc.astype(jnp.bfloat16)[None]
    terms = jnp.stack(encoder_list).astype(jnp.bfloat16)
    section_share = lax.psum_scatter(terms, "section", scatter_dimension=3, tiled=True)
    section_share = section_share.astype(jnp.float32)
    micro, enc_rows_all, examples_all, width_sec = section_share.shape
    row_blocks = section_share.reshape(
        micro, groups, enc_rows_all // groups, examples_all, width_sec
    ).transpose(1, 0, 3, 2, 4)
    received = lax.all_to_all(row_blocks, "dp", 0, 0, tiled=True)
    grad_encoder = jnp.sum(received, axis=0)
    return (attention, query_grads, key_grads, value_grads, grad_encoder)


def solution(mesh):
    placed = (
        P(None, None, "dp", "section"),
        P(),
        P(),
        P("section", None, None, None, "dp"),
        P("section", None, None, None, "dp"),
        P("section", None, "dp"),
        P("section", None, "dp"),
    )
    return jax.shard_map(
        body,
        mesh=mesh,
        in_specs=placed,
        out_specs=(
            P("section", None, None, None, "dp"),
            P("section", None, None, None, "dp"),
            P("section", None, "dp"),
            P("section", None, "dp"),
            P(None, None, "dp", "section"),
        ),
        check_vma=False,
    )
```

```python
import jax
import jax.numpy as jnp
from jax import lax
from jax.sharding import PartitionSpec as P

HD = 256
BLOCK = 128
ENC_BLOCKS = 2
MICRO = 2


NEG_FILL = -1e30


def attend(query_rows, key_rows, value_rows, cotan_rows, key_valid, query_valid):
    score_scale = HD ** (-0.5)
    scores = (
        jnp.einsum("eqhd,ekhd->ehqk", query_rows, key_rows, preferred_element_type=jnp.float32)
        * score_scale
    )
    scores = jnp.where(key_valid[:, None, None, :], scores, NEG_FILL)
    largest = jnp.max(scores, axis=-1, keepdims=True)
    weights = jnp.exp(scores - largest)
    probs = weights / jnp.sum(weights, axis=-1, keepdims=True)
    probs_low = probs.astype(jnp.bfloat16)
    attended = jnp.einsum(
        "ehqk,ekhd->eqhd", probs_low, value_rows, preferred_element_type=jnp.float32
    )
    attended = jnp.where(query_valid[:, :, None, None], attended, 0.0).astype(jnp.bfloat16)
    cotan_kept = jnp.where(query_valid[:, :, None, None], cotan_rows, jnp.zeros_like(cotan_rows))
    grad_value = jnp.einsum(
        "ehqk,eqhd->ekhd", probs_low, cotan_kept, preferred_element_type=jnp.float32
    ).astype(jnp.bfloat16)
    grad_probs = jnp.einsum(
        "eqhd,ekhd->ehqk", cotan_kept, value_rows, preferred_element_type=jnp.float32
    )
    inner_sum = jnp.sum(probs * grad_probs, axis=-1, keepdims=True)
    grad_scores = (probs * (grad_probs - inner_sum) * score_scale).astype(jnp.bfloat16)
    grad_query = jnp.einsum(
        "ehqk,ekhd->eqhd", grad_scores, key_rows, preferred_element_type=jnp.float32
    ).astype(jnp.bfloat16)
    grad_key = jnp.einsum(
        "ehqk,eqhd->ekhd", grad_scores, query_rows, preferred_element_type=jnp.float32
    ).astype(jnp.bfloat16)
    return (attended, grad_query, grad_key, grad_value)


def body(encoder_out, encoder_len, decoder_len, queries, cotangent, key_weight, value_weight):
    key_mat = key_weight[0]
    value_mat = value_weight[0]
    width_dev = key_mat.shape[1]
    heads_dev = width_dev // HD
    enc_rows = ENC_BLOCKS * BLOCK
    dec_rows = queries.shape[3]
    examples = queries.shape[2]
    rows_dev = enc_rows // lax.axis_size("dp")
    key_positions = jnp.arange(enc_rows, dtype=jnp.int32)
    query_positions = jnp.arange(dec_rows, dtype=jnp.int32)
    key_acc = jnp.zeros(key_mat.shape, jnp.float32)
    value_acc = jnp.zeros(value_mat.shape, jnp.float32)
    attn_list, query_list, encoder_list = ([], [], [])
    groups = lax.axis_size("dp")
    copies = jnp.broadcast_to(encoder_out[None], (groups,) + encoder_out.shape)
    from_each = lax.all_to_all(copies, "dp", 0, 0, tiled=True)
    tall_enc = jnp.moveaxis(from_each, 0, 2).reshape(
        encoder_out.shape[:2] + (groups * encoder_out.shape[2], encoder_out.shape[3])
    )
    gathered_enc = lax.all_gather(tall_enc, "section", axis=3, tiled=True)
    for micro_idx in range(MICRO):
        whole_enc = gathered_enc[micro_idx]
        key_rows = jnp.einsum(
            "ekd,dc->ekc", whole_enc, key_mat, preferred_element_type=jnp.float32
        ).astype(jnp.bfloat16)
        value_rows = jnp.einsum(
            "ekd,dc->ekc", whole_enc, value_mat, preferred_element_type=jnp.float32
        ).astype(jnp.bfloat16)
        key_valid = key_positions[None, :] < (BLOCK * encoder_len[micro_idx])[:, None]
        query_valid = query_positions[None, :] < (BLOCK * decoder_len[micro_idx])[:, None]
        attended, grad_query, grad_key, grad_value = attend(
            queries[0, micro_idx].reshape(examples, dec_rows, heads_dev, HD),
            key_rows.reshape(examples, enc_rows, heads_dev, HD),
            value_rows.reshape(examples, enc_rows, heads_dev, HD),
            cotangent[0, micro_idx].reshape(examples, dec_rows, heads_dev, HD),
            key_valid,
            query_valid,
        )
        key_flat = grad_key.reshape(examples, enc_rows, width_dev)
        value_flat = grad_value.reshape(examples, enc_rows, width_dev)
        key_acc = key_acc + jnp.einsum(
            "ekd,ekc->dc", whole_enc, key_flat, preferred_element_type=jnp.float32
        )
        value_acc = value_acc + jnp.einsum(
            "ekd,ekc->dc", whole_enc, value_flat, preferred_element_type=jnp.float32
        )

        def head_term(first_row, row_count, key_flat=key_flat, value_flat=value_flat):
            return jnp.einsum(
                "ekc,dc->ked", key_flat, key_mat, preferred_element_type=jnp.float32
            ) + jnp.einsum("ekc,dc->ked", value_flat, value_mat, preferred_element_type=jnp.float32)

        encoder_list.append(head_term(jnp.int32(0), lax.axis_size("dp") * rows_dev))
        attn_list.append(attended.reshape(examples, dec_rows, width_dev))
        query_list.append(grad_query.reshape(examples, dec_rows, width_dev))
    attention = jnp.stack(attn_list)[None]
    query_grads = jnp.stack(query_list)[None]
    key_grads = key_acc.astype(jnp.bfloat16)[None]
    value_grads = value_acc.astype(jnp.bfloat16)[None]
    terms = jnp.stack(encoder_list).astype(jnp.bfloat16)
    sections = lax.axis_size("section")
    feature_blocks = jnp.moveaxis(
        terms.reshape(terms.shape[:3] + (sections, terms.shape[3] // sections)), 3, 0
    )
    from_sections = lax.all_to_all(feature_blocks, "section", 0, 0, tiled=True)
    section_share = jnp.sum(from_sections.astype(jnp.float32), axis=0)
    micro, enc_rows_all, examples_all, width_sec = section_share.shape
    row_blocks = section_share.reshape(
        micro, groups, enc_rows_all // groups, examples_all, width_sec
    ).transpose(1, 0, 3, 2, 4)
    received = lax.all_to_all(row_blocks, "dp", 0, 0, tiled=True)
    grad_encoder = jnp.sum(received, axis=0)
    return (attention, query_grads, key_grads, value_grads, grad_encoder)


def solution(mesh):
    placed = (
        P(None, None, "dp", "section"),
        P(),
        P(),
        P("section", None, None, None, "dp"),
        P("section", None, None, None, "dp"),
        P("section", None, "dp"),
        P("section", None, "dp"),
    )
    return jax.shard_map(
        body,
        mesh=mesh,
        in_specs=placed,
        out_specs=(
            P("section", None, None, None, "dp"),
            P("section", None, None, None, "dp"),
            P("section", None, "dp"),
            P("section", None, "dp"),
            P(None, None, "dp", "section"),
        ),
        check_vma=False,
    )
```

```python
import jax
import jax.numpy as jnp
from jax import lax
from jax.sharding import PartitionSpec as P

HD = 256
BLOCK = 128
ENC_BLOCKS = 2
MICRO = 2


NEG_FILL = -1e30


def attend(query_rows, key_rows, value_rows, cotan_rows, key_valid, query_valid):
    score_scale = HD ** (-0.5)
    scores = (
        jnp.einsum("eqhd,ekhd->ehqk", query_rows, key_rows, preferred_element_type=jnp.float32)
        * score_scale
    )
    scores = jnp.where(key_valid[:, None, None, :], scores, NEG_FILL)
    largest = jnp.max(scores, axis=-1, keepdims=True)
    weights = jnp.exp(scores - largest)
    probs = weights / jnp.sum(weights, axis=-1, keepdims=True)
    probs_low = probs.astype(jnp.bfloat16)
    attended = jnp.einsum(
        "ehqk,ekhd->eqhd", probs_low, value_rows, preferred_element_type=jnp.float32
    )
    attended = jnp.where(query_valid[:, :, None, None], attended, 0.0).astype(jnp.bfloat16)
    cotan_kept = jnp.where(query_valid[:, :, None, None], cotan_rows, jnp.zeros_like(cotan_rows))
    grad_value = jnp.einsum(
        "ehqk,eqhd->ekhd", probs_low, cotan_kept, preferred_element_type=jnp.float32
    ).astype(jnp.bfloat16)
    grad_probs = jnp.einsum(
        "eqhd,ekhd->ehqk", cotan_kept, value_rows, preferred_element_type=jnp.float32
    )
    inner_sum = jnp.sum(probs * grad_probs, axis=-1, keepdims=True)
    grad_scores = (probs * (grad_probs - inner_sum) * score_scale).astype(jnp.bfloat16)
    grad_query = jnp.einsum(
        "ehqk,ekhd->eqhd", grad_scores, key_rows, preferred_element_type=jnp.float32
    ).astype(jnp.bfloat16)
    grad_key = jnp.einsum(
        "ehqk,eqhd->ekhd", grad_scores, query_rows, preferred_element_type=jnp.float32
    ).astype(jnp.bfloat16)
    return (attended, grad_query, grad_key, grad_value)


def body(encoder_out, encoder_len, decoder_len, queries, cotangent, key_weight, value_weight):
    key_mat = key_weight[0]
    value_mat = value_weight[0]
    width_dev = key_mat.shape[1]
    heads_dev = width_dev // HD
    enc_rows = ENC_BLOCKS * BLOCK
    dec_rows = queries.shape[3]
    examples = queries.shape[2]
    rows_dev = enc_rows // lax.axis_size("dp")
    key_positions = jnp.arange(enc_rows, dtype=jnp.int32)
    query_positions = jnp.arange(dec_rows, dtype=jnp.int32)
    key_acc = jnp.zeros(key_mat.shape, jnp.float32)
    value_acc = jnp.zeros(value_mat.shape, jnp.float32)
    attn_list, query_list, encoder_list = ([], [], [])
    groups = lax.axis_size("dp")
    copies = jnp.broadcast_to(encoder_out[None], (groups,) + encoder_out.shape)
    from_each = lax.all_to_all(copies, "dp", 0, 0, tiled=True)
    tall_enc = jnp.moveaxis(from_each, 0, 2).reshape(
        encoder_out.shape[:2] + (groups * encoder_out.shape[2], encoder_out.shape[3])
    )
    gathered_enc = lax.all_gather(tall_enc, "section", axis=3, tiled=True)
    for micro_idx in range(MICRO):
        whole_enc = gathered_enc[micro_idx]
        key_rows = jnp.einsum(
            "ekd,dc->ekc", whole_enc, key_mat, preferred_element_type=jnp.float32
        ).astype(jnp.bfloat16)
        value_rows = jnp.einsum(
            "ekd,dc->ekc", whole_enc, value_mat, preferred_element_type=jnp.float32
        ).astype(jnp.bfloat16)
        key_valid = key_positions[None, :] < (BLOCK * encoder_len[micro_idx])[:, None]
        query_valid = query_positions[None, :] < (BLOCK * decoder_len[micro_idx])[:, None]
        attended, grad_query, grad_key, grad_value = attend(
            queries[0, micro_idx].reshape(examples, dec_rows, heads_dev, HD),
            key_rows.reshape(examples, enc_rows, heads_dev, HD),
            value_rows.reshape(examples, enc_rows, heads_dev, HD),
            cotangent[0, micro_idx].reshape(examples, dec_rows, heads_dev, HD),
            key_valid,
            query_valid,
        )
        key_flat = grad_key.reshape(examples, enc_rows, width_dev)
        value_flat = grad_value.reshape(examples, enc_rows, width_dev)
        key_acc = key_acc + jnp.einsum(
            "ekd,ekc->dc", whole_enc, key_flat, preferred_element_type=jnp.float32
        )
        value_acc = value_acc + jnp.einsum(
            "ekd,ekc->dc", whole_enc, value_flat, preferred_element_type=jnp.float32
        )

        def head_term(first_row, row_count, key_flat=key_flat, value_flat=value_flat):
            return jnp.einsum(
                "ekc,dc->ked", key_flat, key_mat, preferred_element_type=jnp.float32
            ) + jnp.einsum("ekc,dc->ked", value_flat, value_mat, preferred_element_type=jnp.float32)

        encoder_list.append(head_term(jnp.int32(0), lax.axis_size("dp") * rows_dev))
        attn_list.append(attended.reshape(examples, dec_rows, width_dev))
        query_list.append(grad_query.reshape(examples, dec_rows, width_dev))
    attention = jnp.stack(attn_list)[None]
    query_grads = jnp.stack(query_list)[None]
    key_grads = key_acc.astype(jnp.bfloat16)[None]
    value_grads = value_acc.astype(jnp.bfloat16)[None]
    terms = jnp.stack(encoder_list).astype(jnp.bfloat16)
    micro, enc_rows_all, examples_all, width_all = terms.shape
    groups = lax.axis_size("dp")
    sections = lax.axis_size("section")
    row_blocks = jnp.moveaxis(
        terms.reshape(micro, groups, enc_rows_all // groups, examples_all, width_all), 1, 0
    )
    from_heads = lax.all_to_all(row_blocks, "dp", 0, 0, tiled=True)
    head_share = jnp.sum(from_heads.astype(jnp.float32), axis=0)
    feature_blocks = jnp.moveaxis(
        head_share.reshape(head_share.shape[:3] + (sections, width_all // sections)), 3, 0
    )
    from_sections = lax.all_to_all(feature_blocks, "section", 0, 0, tiled=True)
    grad_encoder = jnp.transpose(jnp.sum(from_sections, axis=0), (0, 2, 1, 3))
    return (attention, query_grads, key_grads, value_grads, grad_encoder)


def solution(mesh):
    placed = (
        P(None, None, "dp", "section"),
        P(),
        P(),
        P("section", None, None, None, "dp"),
        P("section", None, None, None, "dp"),
        P("section", None, "dp"),
        P("section", None, "dp"),
    )
    return jax.shard_map(
        body,
        mesh=mesh,
        in_specs=placed,
        out_specs=(
            P("section", None, None, None, "dp"),
            P("section", None, None, None, "dp"),
            P("section", None, "dp"),
            P("section", None, "dp"),
            P(None, None, "dp", "section"),
        ),
        check_vma=False,
    )
```

```python
import jax
import jax.numpy as jnp
from jax import lax
from jax.sharding import PartitionSpec as P

HD = 256
BLOCK = 128
ENC_BLOCKS = 2
MICRO = 2


NEG_FILL = -1e30


def attend(query_rows, key_rows, value_rows, cotan_rows, key_valid, query_valid):
    score_scale = HD ** (-0.5)
    scores = (
        jnp.einsum("eqhd,ekhd->ehqk", query_rows, key_rows, preferred_element_type=jnp.float32)
        * score_scale
    )
    scores = jnp.where(key_valid[:, None, None, :], scores, NEG_FILL)
    largest = jnp.max(scores, axis=-1, keepdims=True)
    weights = jnp.exp(scores - largest)
    probs = weights / jnp.sum(weights, axis=-1, keepdims=True)
    probs_low = probs.astype(jnp.bfloat16)
    attended = jnp.einsum(
        "ehqk,ekhd->eqhd", probs_low, value_rows, preferred_element_type=jnp.float32
    )
    attended = jnp.where(query_valid[:, :, None, None], attended, 0.0).astype(jnp.bfloat16)
    cotan_kept = jnp.where(query_valid[:, :, None, None], cotan_rows, jnp.zeros_like(cotan_rows))
    grad_value = jnp.einsum(
        "ehqk,eqhd->ekhd", probs_low, cotan_kept, preferred_element_type=jnp.float32
    ).astype(jnp.bfloat16)
    grad_probs = jnp.einsum(
        "eqhd,ekhd->ehqk", cotan_kept, value_rows, preferred_element_type=jnp.float32
    )
    inner_sum = jnp.sum(probs * grad_probs, axis=-1, keepdims=True)
    grad_scores = (probs * (grad_probs - inner_sum) * score_scale).astype(jnp.bfloat16)
    grad_query = jnp.einsum(
        "ehqk,ekhd->eqhd", grad_scores, key_rows, preferred_element_type=jnp.float32
    ).astype(jnp.bfloat16)
    grad_key = jnp.einsum(
        "ehqk,eqhd->ekhd", grad_scores, query_rows, preferred_element_type=jnp.float32
    ).astype(jnp.bfloat16)
    return (attended, grad_query, grad_key, grad_value)


def body(encoder_out, encoder_len, decoder_len, queries, cotangent, key_weight, value_weight):
    key_mat = key_weight[0]
    value_mat = value_weight[0]
    width_dev = key_mat.shape[1]
    heads_dev = width_dev // HD
    enc_rows = ENC_BLOCKS * BLOCK
    dec_rows = queries.shape[3]
    examples = queries.shape[2]
    rows_dev = enc_rows // lax.axis_size("dp")
    key_positions = jnp.arange(enc_rows, dtype=jnp.int32)
    query_positions = jnp.arange(dec_rows, dtype=jnp.int32)
    key_acc = jnp.zeros(key_mat.shape, jnp.float32)
    value_acc = jnp.zeros(value_mat.shape, jnp.float32)
    attn_list, query_list, encoder_list = ([], [], [])
    groups = lax.axis_size("dp")
    copies = jnp.broadcast_to(encoder_out[None], (groups,) + encoder_out.shape)
    from_each = lax.all_to_all(copies, "dp", 0, 0, tiled=True)
    tall_enc = jnp.moveaxis(from_each, 0, 2).reshape(
        encoder_out.shape[:2] + (groups * encoder_out.shape[2], encoder_out.shape[3])
    )
    gathered_enc = lax.all_gather(tall_enc, "section", axis=3, tiled=True)
    for micro_idx in range(MICRO):
        whole_enc = gathered_enc[micro_idx]
        key_rows = jnp.einsum(
            "ekd,dc->ekc", whole_enc, key_mat, preferred_element_type=jnp.float32
        ).astype(jnp.bfloat16)
        value_rows = jnp.einsum(
            "ekd,dc->ekc", whole_enc, value_mat, preferred_element_type=jnp.float32
        ).astype(jnp.bfloat16)
        key_valid = key_positions[None, :] < (BLOCK * encoder_len[micro_idx])[:, None]
        query_valid = query_positions[None, :] < (BLOCK * decoder_len[micro_idx])[:, None]
        attended, grad_query, grad_key, grad_value = attend(
            queries[0, micro_idx].reshape(examples, dec_rows, heads_dev, HD),
            key_rows.reshape(examples, enc_rows, heads_dev, HD),
            value_rows.reshape(examples, enc_rows, heads_dev, HD),
            cotangent[0, micro_idx].reshape(examples, dec_rows, heads_dev, HD),
            key_valid,
            query_valid,
        )
        key_flat = grad_key.reshape(examples, enc_rows, width_dev)
        value_flat = grad_value.reshape(examples, enc_rows, width_dev)
        key_acc = key_acc + jnp.einsum(
            "ekd,ekc->dc", whole_enc, key_flat, preferred_element_type=jnp.float32
        )
        value_acc = value_acc + jnp.einsum(
            "ekd,ekc->dc", whole_enc, value_flat, preferred_element_type=jnp.float32
        )

        def head_term(first_row, row_count, key_flat=key_flat, value_flat=value_flat):
            return jnp.einsum(
                "ekc,dc->ked", key_flat, key_mat, preferred_element_type=jnp.float32
            ) + jnp.einsum("ekc,dc->ked", value_flat, value_mat, preferred_element_type=jnp.float32)

        term = head_term(jnp.int32(0), lax.axis_size("dp") * rows_dev).astype(jnp.bfloat16)
        sections = lax.axis_size("section")
        feature_blocks = jnp.moveaxis(
            term.reshape(term.shape[:2] + (sections, term.shape[2] // sections)), 2, 0
        )
        from_sections = lax.all_to_all(feature_blocks, "section", 0, 0, tiled=True)
        encoder_list.append(jnp.sum(from_sections.astype(jnp.float32), axis=0))
        attn_list.append(attended.reshape(examples, dec_rows, width_dev))
        query_list.append(grad_query.reshape(examples, dec_rows, width_dev))
    attention = jnp.stack(attn_list)[None]
    query_grads = jnp.stack(query_list)[None]
    key_grads = key_acc.astype(jnp.bfloat16)[None]
    value_grads = value_acc.astype(jnp.bfloat16)[None]
    section_share = jnp.stack(encoder_list)
    micro, enc_rows_all, examples_all, width_sec = section_share.shape
    row_blocks = section_share.reshape(
        micro, groups, enc_rows_all // groups, examples_all, width_sec
    ).transpose(1, 0, 3, 2, 4)
    received = lax.all_to_all(row_blocks, "dp", 0, 0, tiled=True)
    grad_encoder = jnp.sum(received, axis=0)
    return (attention, query_grads, key_grads, value_grads, grad_encoder)


def solution(mesh):
    placed = (
        P(None, None, "dp", "section"),
        P(),
        P(),
        P("section", None, None, None, "dp"),
        P("section", None, None, None, "dp"),
        P("section", None, "dp"),
        P("section", None, "dp"),
    )
    return jax.shard_map(
        body,
        mesh=mesh,
        in_specs=placed,
        out_specs=(
            P("section", None, None, None, "dp"),
            P("section", None, None, None, "dp"),
            P("section", None, "dp"),
            P("section", None, "dp"),
            P(None, None, "dp", "section"),
        ),
        check_vma=False,
    )
```

```python
import jax
import jax.numpy as jnp
from jax import lax
from jax.sharding import PartitionSpec as P

HD = 256
BLOCK = 128
ENC_BLOCKS = 2
MICRO = 2


NEG_FILL = -1e30


def attend(query_rows, key_rows, value_rows, cotan_rows, key_valid, query_valid):
    score_scale = HD ** (-0.5)
    scores = (
        jnp.einsum("eqhd,ekhd->ehqk", query_rows, key_rows, preferred_element_type=jnp.float32)
        * score_scale
    )
    scores = jnp.where(key_valid[:, None, None, :], scores, NEG_FILL)
    largest = jnp.max(scores, axis=-1, keepdims=True)
    weights = jnp.exp(scores - largest)
    probs = weights / jnp.sum(weights, axis=-1, keepdims=True)
    probs_low = probs.astype(jnp.bfloat16)
    attended = jnp.einsum(
        "ehqk,ekhd->eqhd", probs_low, value_rows, preferred_element_type=jnp.float32
    )
    attended = jnp.where(query_valid[:, :, None, None], attended, 0.0).astype(jnp.bfloat16)
    cotan_kept = jnp.where(query_valid[:, :, None, None], cotan_rows, jnp.zeros_like(cotan_rows))
    grad_value = jnp.einsum(
        "ehqk,eqhd->ekhd", probs_low, cotan_kept, preferred_element_type=jnp.float32
    ).astype(jnp.bfloat16)
    grad_probs = jnp.einsum(
        "eqhd,ekhd->ehqk", cotan_kept, value_rows, preferred_element_type=jnp.float32
    )
    inner_sum = jnp.sum(probs * grad_probs, axis=-1, keepdims=True)
    grad_scores = (probs * (grad_probs - inner_sum) * score_scale).astype(jnp.bfloat16)
    grad_query = jnp.einsum(
        "ehqk,ekhd->eqhd", grad_scores, key_rows, preferred_element_type=jnp.float32
    ).astype(jnp.bfloat16)
    grad_key = jnp.einsum(
        "ehqk,eqhd->ekhd", grad_scores, query_rows, preferred_element_type=jnp.float32
    ).astype(jnp.bfloat16)
    return (attended, grad_query, grad_key, grad_value)


def body(encoder_out, encoder_len, decoder_len, queries, cotangent, key_weight, value_weight):
    key_mat = key_weight[0]
    value_mat = value_weight[0]
    width_dev = key_mat.shape[1]
    heads_dev = width_dev // HD
    enc_rows = ENC_BLOCKS * BLOCK
    dec_rows = queries.shape[3]
    examples = queries.shape[2]
    rows_dev = enc_rows // lax.axis_size("dp")
    key_positions = jnp.arange(enc_rows, dtype=jnp.int32)
    query_positions = jnp.arange(dec_rows, dtype=jnp.int32)
    key_acc = jnp.zeros(key_mat.shape, jnp.float32)
    value_acc = jnp.zeros(value_mat.shape, jnp.float32)
    attn_list, query_list, encoder_list = ([], [], [])
    groups = lax.axis_size("dp")
    copies = jnp.broadcast_to(encoder_out[None], (groups,) + encoder_out.shape)
    from_each = lax.all_to_all(copies, "dp", 0, 0, tiled=True)
    tall_enc = jnp.moveaxis(from_each, 0, 2).reshape(
        encoder_out.shape[:2] + (groups * encoder_out.shape[2], encoder_out.shape[3])
    )
    gathered_enc = [
        lax.all_gather(tall_enc[micro_idx], "section", axis=2, tiled=True)
        for micro_idx in range(MICRO)
    ]
    for micro_idx in range(MICRO):
        whole_enc = gathered_enc[micro_idx]
        key_rows = jnp.einsum(
            "ekd,dc->ekc", whole_enc, key_mat, preferred_element_type=jnp.float32
        ).astype(jnp.bfloat16)
        value_rows = jnp.einsum(
            "ekd,dc->ekc", whole_enc, value_mat, preferred_element_type=jnp.float32
        ).astype(jnp.bfloat16)
        key_valid = key_positions[None, :] < (BLOCK * encoder_len[micro_idx])[:, None]
        query_valid = query_positions[None, :] < (BLOCK * decoder_len[micro_idx])[:, None]
        attended, grad_query, grad_key, grad_value = attend(
            queries[0, micro_idx].reshape(examples, dec_rows, heads_dev, HD),
            key_rows.reshape(examples, enc_rows, heads_dev, HD),
            value_rows.reshape(examples, enc_rows, heads_dev, HD),
            cotangent[0, micro_idx].reshape(examples, dec_rows, heads_dev, HD),
            key_valid,
            query_valid,
        )
        key_flat = grad_key.reshape(examples, enc_rows, width_dev)
        value_flat = grad_value.reshape(examples, enc_rows, width_dev)
        key_acc = key_acc + jnp.einsum(
            "ekd,ekc->dc", whole_enc, key_flat, preferred_element_type=jnp.float32
        )
        value_acc = value_acc + jnp.einsum(
            "ekd,ekc->dc", whole_enc, value_flat, preferred_element_type=jnp.float32
        )

        def head_term(first_row, row_count, key_flat=key_flat, value_flat=value_flat):
            return jnp.einsum(
                "ekc,dc->ked", key_flat, key_mat, preferred_element_type=jnp.float32
            ) + jnp.einsum("ekc,dc->ked", value_flat, value_mat, preferred_element_type=jnp.float32)

        term = head_term(jnp.int32(0), lax.axis_size("dp") * rows_dev).astype(jnp.bfloat16)
        sections = lax.axis_size("section")
        feature_blocks = jnp.moveaxis(
            term.reshape(term.shape[:2] + (sections, term.shape[2] // sections)), 2, 0
        )
        from_sections = lax.all_to_all(feature_blocks, "section", 0, 0, tiled=True)
        encoder_list.append(jnp.sum(from_sections.astype(jnp.float32), axis=0))
        attn_list.append(attended.reshape(examples, dec_rows, width_dev))
        query_list.append(grad_query.reshape(examples, dec_rows, width_dev))
    attention = jnp.stack(attn_list)[None]
    query_grads = jnp.stack(query_list)[None]
    key_grads = key_acc.astype(jnp.bfloat16)[None]
    value_grads = value_acc.astype(jnp.bfloat16)[None]
    section_share = jnp.stack(encoder_list)
    micro, enc_rows_all, examples_all, width_sec = section_share.shape
    row_blocks = section_share.reshape(
        micro, groups, enc_rows_all // groups, examples_all, width_sec
    ).transpose(1, 0, 3, 2, 4)
    received = lax.all_to_all(row_blocks, "dp", 0, 0, tiled=True)
    grad_encoder = jnp.sum(received, axis=0)
    return (attention, query_grads, key_grads, value_grads, grad_encoder)


def solution(mesh):
    placed = (
        P(None, None, "dp", "section"),
        P(),
        P(),
        P("section", None, None, None, "dp"),
        P("section", None, None, None, "dp"),
        P("section", None, "dp"),
        P("section", None, "dp"),
    )
    return jax.shard_map(
        body,
        mesh=mesh,
        in_specs=placed,
        out_specs=(
            P("section", None, None, None, "dp"),
            P("section", None, None, None, "dp"),
            P("section", None, "dp"),
            P("section", None, "dp"),
            P(None, None, "dp", "section"),
        ),
        check_vma=False,
    )
```

```python
import jax
import jax.numpy as jnp
from jax import lax
from jax.sharding import PartitionSpec as P

HD = 256
BLOCK = 128
ENC_BLOCKS = 2
MICRO = 2


NEG_FILL = -1e30


def attend(query_rows, key_rows, value_rows, cotan_rows, key_valid, query_valid):
    score_scale = HD ** (-0.5)
    scores = (
        jnp.einsum("eqhd,ekhd->ehqk", query_rows, key_rows, preferred_element_type=jnp.float32)
        * score_scale
    )
    scores = jnp.where(key_valid[:, None, None, :], scores, NEG_FILL)
    largest = jnp.max(scores, axis=-1, keepdims=True)
    weights = jnp.exp(scores - largest)
    probs = weights / jnp.sum(weights, axis=-1, keepdims=True)
    probs_low = probs.astype(jnp.bfloat16)
    attended = jnp.einsum(
        "ehqk,ekhd->eqhd", probs_low, value_rows, preferred_element_type=jnp.float32
    )
    attended = jnp.where(query_valid[:, :, None, None], attended, 0.0).astype(jnp.bfloat16)
    cotan_kept = jnp.where(query_valid[:, :, None, None], cotan_rows, jnp.zeros_like(cotan_rows))
    grad_value = jnp.einsum(
        "ehqk,eqhd->ekhd", probs_low, cotan_kept, preferred_element_type=jnp.float32
    ).astype(jnp.bfloat16)
    grad_probs = jnp.einsum(
        "eqhd,ekhd->ehqk", cotan_kept, value_rows, preferred_element_type=jnp.float32
    )
    inner_sum = jnp.sum(probs * grad_probs, axis=-1, keepdims=True)
    grad_scores = (probs * (grad_probs - inner_sum) * score_scale).astype(jnp.bfloat16)
    grad_query = jnp.einsum(
        "ehqk,ekhd->eqhd", grad_scores, key_rows, preferred_element_type=jnp.float32
    ).astype(jnp.bfloat16)
    grad_key = jnp.einsum(
        "ehqk,eqhd->ekhd", grad_scores, query_rows, preferred_element_type=jnp.float32
    ).astype(jnp.bfloat16)
    return (attended, grad_query, grad_key, grad_value)


def body(encoder_out, encoder_len, decoder_len, queries, cotangent, key_weight, value_weight):
    key_mat = key_weight[0]
    value_mat = value_weight[0]
    width_dev = key_mat.shape[1]
    heads_dev = width_dev // HD
    enc_rows = ENC_BLOCKS * BLOCK
    dec_rows = queries.shape[3]
    examples = queries.shape[2]
    rows_dev = enc_rows // lax.axis_size("dp")
    key_positions = jnp.arange(enc_rows, dtype=jnp.int32)
    query_positions = jnp.arange(dec_rows, dtype=jnp.int32)
    key_acc = jnp.zeros(key_mat.shape, jnp.float32)
    value_acc = jnp.zeros(value_mat.shape, jnp.float32)
    attn_list, query_list, encoder_list = ([], [], [])
    groups = lax.axis_size("dp")
    copies = jnp.broadcast_to(encoder_out[None], (groups,) + encoder_out.shape)
    from_each = lax.all_to_all(copies, "dp", 0, 0, tiled=True)
    tall_enc = jnp.moveaxis(from_each, 0, 2).reshape(
        encoder_out.shape[:2] + (groups * encoder_out.shape[2], encoder_out.shape[3])
    )
    gathered_enc = lax.all_gather(tall_enc, "section", axis=3, tiled=True)
    for micro_idx in range(MICRO):
        whole_enc = gathered_enc[micro_idx]
        key_rows = jnp.einsum(
            "ekd,dc->ekc", whole_enc, key_mat, preferred_element_type=jnp.float32
        ).astype(jnp.bfloat16)
        value_rows = jnp.einsum(
            "ekd,dc->ekc", whole_enc, value_mat, preferred_element_type=jnp.float32
        ).astype(jnp.bfloat16)
        key_valid = key_positions[None, :] < (BLOCK * encoder_len[micro_idx])[:, None]
        query_valid = query_positions[None, :] < (BLOCK * decoder_len[micro_idx])[:, None]
        attended, grad_query, grad_key, grad_value = attend(
            queries[0, micro_idx].reshape(examples, dec_rows, heads_dev, HD),
            key_rows.reshape(examples, enc_rows, heads_dev, HD),
            value_rows.reshape(examples, enc_rows, heads_dev, HD),
            cotangent[0, micro_idx].reshape(examples, dec_rows, heads_dev, HD),
            key_valid,
            query_valid,
        )
        key_flat = grad_key.reshape(examples, enc_rows, width_dev)
        value_flat = grad_value.reshape(examples, enc_rows, width_dev)
        key_acc = key_acc + jnp.einsum(
            "ekd,ekc->dc", whole_enc, key_flat, preferred_element_type=jnp.float32
        )
        value_acc = value_acc + jnp.einsum(
            "ekd,ekc->dc", whole_enc, value_flat, preferred_element_type=jnp.float32
        )

        sections = lax.axis_size("section")
        key_blocks = key_mat.reshape(sections, key_mat.shape[0] // sections, width_dev)
        value_blocks = value_mat.reshape(sections, value_mat.shape[0] // sections, width_dev)
        feature_blocks = (
            jnp.einsum("ekc,fdc->fked", key_flat, key_blocks, preferred_element_type=jnp.float32)
            + jnp.einsum(
                "ekc,fdc->fked", value_flat, value_blocks, preferred_element_type=jnp.float32
            )
        ).astype(jnp.bfloat16)
        from_sections = lax.all_to_all(feature_blocks, "section", 0, 0, tiled=True)
        encoder_list.append(jnp.sum(from_sections.astype(jnp.float32), axis=0))
        attn_list.append(attended.reshape(examples, dec_rows, width_dev))
        query_list.append(grad_query.reshape(examples, dec_rows, width_dev))
    attention = jnp.stack(attn_list)[None]
    query_grads = jnp.stack(query_list)[None]
    key_grads = key_acc.astype(jnp.bfloat16)[None]
    value_grads = value_acc.astype(jnp.bfloat16)[None]
    section_share = jnp.stack(encoder_list)
    micro, enc_rows_all, examples_all, width_sec = section_share.shape
    row_blocks = section_share.reshape(
        micro, groups, enc_rows_all // groups, examples_all, width_sec
    ).transpose(1, 0, 3, 2, 4)
    received = lax.all_to_all(row_blocks, "dp", 0, 0, tiled=True)
    grad_encoder = jnp.sum(received, axis=0)
    return (attention, query_grads, key_grads, value_grads, grad_encoder)


def solution(mesh):
    placed = (
        P(None, None, "dp", "section"),
        P(),
        P(),
        P("section", None, None, None, "dp"),
        P("section", None, None, None, "dp"),
        P("section", None, "dp"),
        P("section", None, "dp"),
    )
    return jax.shard_map(
        body,
        mesh=mesh,
        in_specs=placed,
        out_specs=(
            P("section", None, None, None, "dp"),
            P("section", None, None, None, "dp"),
            P("section", None, "dp"),
            P("section", None, "dp"),
            P(None, None, "dp", "section"),
        ),
        check_vma=False,
    )
```
